256 devices in a mesh: prow: 8 (over x_lo, y), pcol: 32 (over x_hi, z, core).
Axes of the slice: x: 4 (x_hi: 2, x_lo: 2; x = x_hi * 2 + x_lo), y: 4, z: 8, core: 2. Of those that a mesh axis runs over, the one named last changes fastest.
Arguments:
- ancestor_inv: bfloat16 [24576, 24576], P('pcol', 'prow'), as said below
- tile_pattern: int32 [192, 192], P('pcol', 'prow'), may hold values from 0 to 1, as said below
- factor_block: bfloat16 [3, 24576, 256], P(None, 'pcol'), may hold values from -0.47851562 to 0.47851562
- row_blocks: int32 [3, 96], replicated, may hold values from 0 to 191, as said below
- diag_base: float32 [3, 256, 256], replicated, may hold values from -6 to 6
Outputs:
- ainv_col: bfloat16 [3, 24576, 256], P(None, 'pcol')
- ainv_row: bfloat16 [3, 256, 24576], P(None, None, 'prow')
- ainv_diag: float32 [3, 256, 256], replicated
The draws below stay inside these ranges and needn't reach their ends.
Inputs may be any that keep to these rules, and one draw needn't show every extreme that they name: ancestor_inv is symmetric. `tile_pattern`: symmetric, with ones on the diagonal. `row_blocks`: each row is strictly increasing, begins with 0 and ends with 191.
All inputs are finite; a program needn't handle non-finite values.
Results may differ from the reference program's by a relative error of at most 0.005.
Values may be sent and summed in bfloat16 or wider, within the bound.
No kernel may reach another device: no remote copies, remote signals or barrier semaphores. Data moves between devices by JAX's collectives and lax.ppermute only.
A program may use at most 64 MiB of HBM per device.

```python
import jax
import jax.numpy as jnp
from jax import lax

BLK = 128
NBLK = 192
SUPER_W = 256
SUPERS = 3
STRUCT = 96
ORDER = 24576


def draw_ancestor_inv(key, part):
    base = jax.random.truncated_normal(key, -4.0, 4.0, (ORDER, ORDER), jnp.float32)
    scale = 0.85 * ORDER ** (-0.25)
    return ((base + base.T) * scale).astype(jnp.bfloat16)


def draw_tile_pattern(key, part):
    picks = jax.random.randint(key, (NBLK, NBLK), 0, 1000)
    present = (picks < 452).astype(jnp.int32)
    present = jnp.maximum(present, present.T)
    return jnp.maximum(present, jnp.eye(NBLK, dtype=jnp.int32))


def draw_row_blocks(key, part):
    keys = jax.random.split(key, SUPERS)

    def one_list(subkey):
        chosen = jax.random.permutation(subkey, NBLK - 2)[:STRUCT - 2].astype(jnp.int32) + 1
        endpoints = jnp.array([0, NBLK - 1], dtype=jnp.int32)
        return jnp.sort(jnp.concatenate([endpoints, chosen]))
    return jax.vmap(one_list)(keys)


def levels(own_key, shape, shards, low, largest):
    def one(dim, parts):
        heights = jax.random.uniform(jax.random.fold_in(jax.random.fold_in(own_key, 6), dim), (parts,), jnp.float32, low / len(shards), largest / len(shards))
        return jnp.repeat(jnp.exp(heights), shape[dim] // parts).reshape((-1,) + (1,) * (len(shape) - dim - 1))

    level = one(*shards[0])
    for cut in shards[1:]:
        level = level * one(*cut)
    return level


def noise(rng, dims, scale, reach, cuts=(), kind=jnp.bfloat16):
    values = scale * jax.random.normal(rng, dims, jnp.float32)
    if cuts:
        values = values * levels(rng, dims, cuts, -0.22, 0.18)
    return jnp.clip(values, -reach, reach).astype(kind)


def setup_inputs(seed: int = 0) -> dict:
    arg_keys = jax.random.split(jax.random.key(seed), 6)
    ancestor_inv = draw_ancestor_inv(jax.random.fold_in(arg_keys[5], 71), 0)
    tile_pattern = draw_tile_pattern(jax.random.fold_in(arg_keys[5], 71), 0)
    factor_block = noise(arg_keys[2], (SUPERS, ORDER, SUPER_W), (ORDER ** -0.25), 0.47851562, ((1, 32),))
    row_blocks = draw_row_blocks(jax.random.fold_in(arg_keys[5], 71), 0)
    diag_base = noise(arg_keys[4], (SUPERS, SUPER_W, SUPER_W), 1.0, 6.0, (), jnp.float32)
    return {"ancestor_inv": ancestor_inv, "tile_pattern": tile_pattern, "factor_block": factor_block, "row_blocks": row_blocks, "diag_base": diag_base}


def reference(ancestor_inv, tile_pattern, factor_block, row_blocks, diag_base):
    blocks = jnp.arange(NBLK, dtype=jnp.int32)
    structure = jnp.any(row_blocks[:, :, None] == blocks[None, None, :], axis=1)
    row_sel = jnp.repeat(structure.astype(jnp.float32), BLK, axis=1)
    factor = factor_block * row_sel[:, :, None].astype(jnp.bfloat16)
    flat_factor = jnp.transpose(factor, (1, 0, 2)).reshape(ORDER, SUPERS * SUPER_W)
    stripes = ancestor_inv.reshape(NBLK, BLK, ORDER)

    def stripe_product(packed):
        stripe, pattern_row = packed
        widened = jnp.repeat(pattern_row.astype(jnp.bfloat16), BLK)
        return jnp.dot(stripe * widened[None, :], flat_factor, preferred_element_type=jnp.float32)

    product = lax.map(stripe_product, (stripes, tile_pattern))
    product = jnp.transpose(product.reshape(ORDER, SUPERS, SUPER_W), (1, 0, 2))
    col_exact = -product * row_sel[:, :, None]
    ainv_col = col_exact.astype(jnp.bfloat16)
    ainv_row = jnp.transpose(ainv_col, (0, 2, 1))
    ainv_diag = diag_base - jnp.einsum("sik,sil->skl", factor.astype(jnp.float32), col_exact.astype(jnp.float32))
    return ainv_col, ainv_row, ainv_diag
```

```python
import jax
import jax.numpy as jnp
from jax import lax
from jax.sharding import Mesh
from jax.sharding import PartitionSpec as P

BLK = 128
COLS = ("pg", "pr")
ALL = ("prow", "pg", "pr")


def expand_tiles(pattern):
    tile_rows, tile_cols = pattern.shape
    widened = jnp.broadcast_to(
        pattern.astype(jnp.bfloat16)[:, None, :, None], (tile_rows, BLK, tile_cols, BLK)
    )
    return widened.reshape(tile_rows * BLK, tile_cols * BLK)


def structure_rows(row_blocks, row_start, how_many):
    row_ids = row_start + jnp.arange(how_many, dtype=jnp.int32)
    matches = row_blocks[:, None, :] == (row_ids // BLK)[None, :, None]
    return jnp.any(matches, axis=2).astype(jnp.float32)


def swap_perm(n_row, n_grp, n_sub):
    pairs = []
    for q in range(n_row):
        for g in range(n_grp):
            for r in range(n_sub):
                pairs.append(((q * n_grp + g) * n_sub + r, (g * n_grp + q) * n_sub + r))
    return pairs


def gather_cols(block, perm):
    moved = lax.ppermute(block, ALL, perm)
    return lax.all_gather(moved, "pr", axis=0, tiled=False)


def shards(ancestor_inv, tile_pattern, factor_block, row_blocks, diag_base):
    col_rows = ancestor_inv.shape[0]
    n_row = lax.axis_size("prow")
    n_grp = lax.axis_size("pg")
    n_sub = lax.axis_size("pr")
    perm = swap_perm(n_row, n_grp, n_sub)
    supers, _, kwidth = factor_block.shape
    pcol_idx = lax.axis_index("pg") * n_sub + lax.axis_index("pr")
    inverse_tiles = ancestor_inv * expand_tiles(tile_pattern)
    own_sel = structure_rows(row_blocks, pcol_idx * col_rows, col_rows)
    local_lower = factor_block * own_sel[:, :, None].astype(jnp.bfloat16)
    lower_cols = gather_cols(local_lower, perm)
    tiles4 = inverse_tiles.reshape(col_rows, n_sub, col_rows)
    partial = jnp.einsum(
        "irj,rsjk->sik", tiles4, lower_cols, preferred_element_type=jnp.float32
    )
    summed = lax.psum(partial, "prow")
    col_exact = -summed * own_sel[:, :, None]
    column = col_exact.astype(jnp.bfloat16)
    column_cols = gather_cols(column, perm)
    row_out = jnp.transpose(column_cols, (1, 3, 0, 2)).reshape(supers, kwidth, n_sub * col_rows)
    contrib = jnp.einsum(
        "rsjk,rsjl->skl", lower_cols, column_cols, preferred_element_type=jnp.float32
    )
    diagonal = diag_base - lax.psum(contrib, "prow")
    return (column, row_out, diagonal)


def solution(mesh):
    n_row, n_col = mesh.devices.shape
    n_sub = n_col // n_row
    split = Mesh(mesh.devices.reshape(n_row, n_row, n_sub), ALL)
    in_specs = (P(COLS, "prow"), P(COLS, "prow"), P(None, COLS, None), P(), P())
    out_specs = (P(None, COLS, None), P(None, None, "prow"), P())
    return jax.shard_map(shards, mesh=split, in_specs=in_specs, out_specs=out_specs, check_vma=False)
```

```python
import jax
import jax.numpy as jnp
from jax import lax
from jax.sharding import Mesh
from jax.sharding import PartitionSpec as P

BLK = 128
COLS = ("pg", "pr")
ALL = ("prow", "pg", "pr")


def expand_tiles(pattern):
    tile_rows, tile_cols = pattern.shape
    widened = jnp.broadcast_to(
        pattern.astype(jnp.bfloat16)[:, None, :, None], (tile_rows, BLK, tile_cols, BLK)
    )
    return widened.reshape(tile_rows * BLK, tile_cols * BLK)


def structure_rows(row_blocks, row_start, how_many):
    row_ids = row_start + jnp.arange(how_many, dtype=jnp.int32)
    matches = row_blocks[:, None, :] == (row_ids // BLK)[None, :, None]
    return jnp.any(matches, axis=2).astype(jnp.float32)


def index_of(n_row, n_grp, n_sub, q, g, r):
    return (q * n_grp + g) * n_sub + r


def swap_perm(n_row, n_grp, n_sub):
    return [
        (index_of(n_row, n_grp, n_sub, q, g, r), index_of(n_row, n_grp, n_sub, g, q, r))
        for q in range(n_row) for g in range(n_grp) for r in range(n_sub)
    ]


def flip_perm(n_row, n_grp, n_sub, bit):
    return [
        (index_of(n_row, n_grp, n_sub, q, g, r), index_of(n_row, n_grp, n_sub, q, g, r ^ bit))
        for q in range(n_row) for g in range(n_grp) for r in range(n_sub)
    ]


def gather_cols(block, perms):
    swap, far, near = perms
    sub = lax.axis_index("pr")
    high = sub // 2
    low = sub % 2
    mine = lax.ppermute(block, ALL, swap)
    other = lax.ppermute(mine, ALL, far)
    pair = jnp.where(high == 0, jnp.stack([mine, other]), jnp.stack([other, mine]))
    twin = lax.ppermute(pair, ALL, near)
    quad = jnp.where(low == 0, jnp.stack([pair, twin], 1), jnp.stack([twin, pair], 1))
    return quad.reshape((4,) + block.shape)


def shards(ancestor_inv, tile_pattern, factor_block, row_blocks, diag_base):
    col_rows = ancestor_inv.shape[0]
    n_row = lax.axis_size("prow")
    n_grp = lax.axis_size("pg")
    n_sub = lax.axis_size("pr")
    perm = (
        swap_perm(n_row, n_grp, n_sub),
        flip_perm(n_row, n_grp, n_sub, 2),
        flip_perm(n_row, n_grp, n_sub, 1),
    )
    supers, _, kwidth = factor_block.shape
    pcol_idx = lax.axis_index("pg") * n_sub + lax.axis_index("pr")
    inverse_tiles = ancestor_inv * expand_tiles(tile_pattern)
    own_sel = structure_rows(row_blocks, pcol_idx * col_rows, col_rows)
    local_lower = factor_block * own_sel[:, :, None].astype(jnp.bfloat16)
    lower_cols = gather_cols(local_lower, perm)
    tiles4 = inverse_tiles.reshape(col_rows, n_sub, col_rows)
    partial = jnp.einsum(
        "irj,rsjk->sik", tiles4, lower_cols, preferred_element_type=jnp.float32
    )
    summed = lax.psum(partial, "prow")
    col_exact = -summed * own_sel[:, :, None]
    column = col_exact.astype(jnp.bfloat16)
    column_cols = gather_cols(column, perm)
    row_out = jnp.transpose(column_cols, (1, 3, 0, 2)).reshape(supers, kwidth, n_sub * col_rows)
    contrib = jnp.einsum(
        "rsjk,rsjl->skl", lower_cols, column_cols, preferred_element_type=jnp.float32
    )
    diagonal = diag_base - lax.psum(contrib, "prow")
    return (column, row_out, diagonal)


def solution(mesh):
    n_row, n_col = mesh.devices.shape
    n_sub = n_col // n_row
    split = Mesh(mesh.devices.reshape(n_row, n_row, n_sub), ALL)
    in_specs = (P(COLS, "prow"), P(COLS, "prow"), P(None, COLS, None), P(), P())
    out_specs = (P(None, COLS, None), P(None, None, "prow"), P())
    return jax.shard_map(shards, mesh=split, in_specs=in_specs, out_specs=out_specs, check_vma=False)
```

```python
import jax
import jax.numpy as jnp
from jax import lax
from jax.sharding import Mesh
from jax.sharding import PartitionSpec as P

BLK = 128
COLS = ("pg", "pr")
ALL = ("prow", "pg", "pr")


def expand_tiles(pattern):
    tile_rows, tile_cols = pattern.shape
    widened = jnp.broadcast_to(
        pattern.astype(jnp.bfloat16)[:, None, :, None], (tile_rows, BLK, tile_cols, BLK)
    )
    return widened.reshape(tile_rows * BLK, tile_cols * BLK)


def structure_rows(row_blocks, row_start, how_many):
    row_ids = row_start + jnp.arange(how_many, dtype=jnp.int32)
    matches = row_blocks[:, None, :] == (row_ids // BLK)[None, :, None]
    return jnp.any(matches, axis=2).astype(jnp.float32)


def index_of(n_row, n_grp, n_sub, q, g, r):
    return (q * n_grp + g) * n_sub + r


def skew(q, g, n_row):
    side = 4 if n_row % 4 == 0 else 1
    return q - q % side + (g + q) % side


def swap_perm(n_row, n_grp, n_sub):
    return [
        (index_of(n_row, n_grp, n_sub, q, g, r), index_of(n_row, n_grp, n_sub, g, skew(q, g, n_row), r))
        for q in range(n_row) for g in range(n_grp) for r in range(n_sub)
    ]


def flip_perm(n_row, n_grp, n_sub, bit):
    return [
        (index_of(n_row, n_grp, n_sub, q, g, r), index_of(n_row, n_grp, n_sub, q, g, r ^ bit))
        for q in range(n_row) for g in range(n_grp) for r in range(n_sub)
    ]


def gather_cols(block, perms):
    swap, far, near = perms
    sub = lax.axis_index("pr")
    high = sub // 2
    low = sub % 2
    mine = lax.ppermute(block, ALL, swap)
    other = lax.ppermute(mine, ALL, far)
    pair = jnp.where(high == 0, jnp.stack([mine, other]), jnp.stack([other, mine]))
    twin = lax.ppermute(pair, ALL, near)
    quad = jnp.where(low == 0, jnp.stack([pair, twin], 1), jnp.stack([twin, pair], 1))
    return quad.reshape((4,) + block.shape)


def shards(ancestor_inv, tile_pattern, factor_block, row_blocks, diag_base):
    col_rows = ancestor_inv.shape[0]
    n_row = lax.axis_size("prow")
    n_grp = lax.axis_size("pg")
    n_sub = lax.axis_size("pr")
    perm = (
        swap_perm(n_row, n_grp, n_sub),
        flip_perm(n_row, n_grp, n_sub, 2),
        flip_perm(n_row, n_grp, n_sub, 1),
    )
    supers, _, kwidth = factor_block.shape
    pcol_idx = lax.axis_index("pg") * n_sub + lax.axis_index("pr")
    inverse_tiles = ancestor_inv * expand_tiles(tile_pattern)
    own_sel = structure_rows(row_blocks, pcol_idx * col_rows, col_rows)
    local_lower = factor_block * own_sel[:, :, None].astype(jnp.bfloat16)
    lower_cols = gather_cols(local_lower, perm)
    tiles4 = inverse_tiles.reshape(col_rows, n_sub, col_rows)
    partial = jnp.einsum(
        "irj,rsjk->sik", tiles4, lower_cols, preferred_element_type=jnp.float32
    )
    summed = lax.psum(partial, "prow")
    col_exact = -summed * own_sel[:, :, None]
    column = col_exact.astype(jnp.bfloat16)
    column_cols = gather_cols(column, perm)
    row_out = jnp.transpose(column_cols, (1, 3, 0, 2)).reshape(supers, kwidth, n_sub * col_rows)
    contrib = jnp.einsum(
        "rsjk,rsjl->skl", lower_cols, column_cols, preferred_element_type=jnp.float32
    )
    diagonal = diag_base - lax.psum(contrib, "prow")
    return (column, row_out, diagonal)


def solution(mesh):
    n_row, n_col = mesh.devices.shape
    n_sub = n_col // n_row
    split = Mesh(mesh.devices.reshape(n_row, n_row, n_sub), ALL)
    in_specs = (P(COLS, "prow"), P(COLS, "prow"), P(None, COLS, None), P(), P())
    out_specs = (P(None, COLS, None), P(None, None, "prow"), P())
    return jax.shard_map(shards, mesh=split, in_specs=in_specs, out_specs=out_specs, check_vma=False)
```

```python
import jax
import jax.numpy as jnp
from jax import lax
from jax.sharding import Mesh
from jax.sharding import PartitionSpec as P

BLK = 128
COLS = ("pg", "pr")
ALL = ("prow", "pg", "pr")


def expand_tiles(pattern):
    tile_rows, tile_cols = pattern.shape
    widened = jnp.broadcast_to(
        pattern.astype(jnp.bfloat16)[:, None, :, None], (tile_rows, BLK, tile_cols, BLK)
    )
    return widened.reshape(tile_rows * BLK, tile_cols * BLK)


def structure_rows(row_blocks, row_start, how_many):
    row_ids = row_start + jnp.arange(how_many, dtype=jnp.int32)
    matches = row_blocks[:, None, :] == (row_ids // BLK)[None, :, None]
    return jnp.any(matches, axis=2).astype(jnp.float32)


def index_of(n_row, n_grp, n_sub, q, g, r):
    return (q * n_grp + g) * n_sub + r


def skew(q, g, n_row):
    side = 4 if n_row % 4 == 0 else 1
    return q - q % side + (g + q) % side


def swap_perm(n_row, n_grp, n_sub):
    return [
        (index_of(n_row, n_grp, n_sub, q, g, r), index_of(n_row, n_grp, n_sub, g, skew(q, g, n_row), r))
        for q in range(n_row) for g in range(n_grp) for r in range(n_sub)
    ]


def flip_perm(n_row, n_grp, n_sub, bit):
    return [
        (index_of(n_row, n_grp, n_sub, q, g, r), index_of(n_row, n_grp, n_sub, q, g, r ^ bit))
        for q in range(n_row) for g in range(n_grp) for r in range(n_sub)
    ]


def gather_cols(block, perms):
    swap, far, near = perms
    mine = lax.ppermute(block, ALL, swap)
    other = lax.ppermute(mine, ALL, far)
    pair = jnp.stack([mine, other])
    twin = lax.ppermute(pair, ALL, near)
    return jnp.stack([pair, twin])


def flip_if(x, cond, axis):
    return jnp.where(cond, jnp.flip(x, axis), x)


def shards(ancestor_inv, tile_pattern, factor_block, row_blocks, diag_base):
    col_rows, row_cols = ancestor_inv.shape
    n_row = lax.axis_size("prow")
    n_grp = lax.axis_size("pg")
    n_sub = lax.axis_size("pr")
    perm = (
        swap_perm(n_row, n_grp, n_sub),
        flip_perm(n_row, n_grp, n_sub, 2),
        flip_perm(n_row, n_grp, n_sub, 1),
    )
    supers, _, kwidth = factor_block.shape
    width = supers * kwidth
    sub = lax.axis_index("pr")
    zbit = sub // 2 == 1
    kbit = sub % 2 == 1
    pcol_idx = lax.axis_index("pg") * n_sub + sub
    own_sel = structure_rows(row_blocks, pcol_idx * col_rows, col_rows)
    sel_rows = jnp.transpose(own_sel)[:, :, None]
    local_lower = jnp.transpose(factor_block, (1, 0, 2)) * sel_rows.astype(jnp.bfloat16)
    lower_cols = gather_cols(local_lower.reshape(col_rows, width), perm)
    mask = expand_tiles(tile_pattern)
    zint = zbit.astype(jnp.int32)
    kint = kbit.astype(jnp.int32)
    pieces = []
    for a in range(2):
        for b in range(2):
            start = (2 * (zint ^ b) + (kint ^ a)) * col_rows
            pieces.append(
                lax.dynamic_slice_in_dim(ancestor_inv, start, col_rows, 1)
                * lax.dynamic_slice_in_dim(mask, start, col_rows, 1)
            )
    tiles = jnp.concatenate(pieces, axis=1)
    partial = jnp.dot(tiles, lower_cols.reshape(row_cols, width), preferred_element_type=jnp.float32)
    summed = lax.psum(partial, "prow")
    col_exact = -summed.reshape(col_rows, supers, kwidth) * sel_rows
    column = col_exact.astype(jnp.bfloat16)
    column_cols = gather_cols(column.reshape(col_rows, width), perm)
    contrib = jnp.einsum(
        "jsk,jsl->skl",
        lower_cols.reshape(row_cols, supers, kwidth),
        column_cols.reshape(row_cols, supers, kwidth),
        preferred_element_type=jnp.float32,
    )
    diagonal = diag_base - lax.psum(contrib, "prow")
    ordered = flip_if(flip_if(column_cols, kbit, 0), zbit, 1)
    ordered = ordered.reshape(2, 2, col_rows, supers, kwidth)
    row_out = jnp.transpose(ordered, (3, 4, 1, 0, 2)).reshape(supers, kwidth, row_cols)
    return (jnp.transpose(column, (1, 0, 2)), row_out, diagonal)


def solution(mesh):
    n_row, n_col = mesh.devices.shape
    n_sub = n_col // n_row
    split = Mesh(mesh.devices.reshape(n_row, n_row, n_sub), ALL)
    in_specs = (P(COLS, "prow"), P(COLS, "prow"), P(None, COLS, None), P(), P())
    out_specs = (P(None, COLS, None), P(None, None, "prow"), P())
    return jax.shard_map(shards, mesh=split, in_specs=in_specs, out_specs=out_specs, check_vma=False)
```

```python
import jax
import jax.numpy as jnp
from jax import lax
from jax.sharding import Mesh
from jax.sharding import PartitionSpec as P

BLK = 128
COLS = ("pg", "pr")
ALL = ("prow", "pg", "pr")


def expand_tiles(pattern):
    tile_rows, tile_cols = pattern.shape
    widened = jnp.broadcast_to(
        pattern.astype(jnp.bfloat16)[:, None, :, None], (tile_rows, BLK, tile_cols, BLK)
    )
    return widened.reshape(tile_rows * BLK, tile_cols * BLK)


def structure_rows(row_blocks, row_start, how_many):
    row_ids = row_start + jnp.arange(how_many, dtype=jnp.int32)
    matches = row_blocks[:, None, :] == (row_ids // BLK)[None, :, None]
    return jnp.any(matches, axis=2).astype(jnp.float32)


def index_of(n_row, n_grp, n_sub, q, g, r):
    return (q * n_grp + g) * n_sub + r


def skew(q, g, n_row):
    side = 4 if n_row % 4 == 0 else 1
    return q - q % side + (g + q) % side


def swap_perm(n_row, n_grp, n_sub):
    return [
        (index_of(n_row, n_grp, n_sub, q, g, r), index_of(n_row, n_grp, n_sub, g, skew(q, g, n_row), r))
        for q in range(n_row) for g in range(n_grp) for r in range(n_sub)
    ]


def flip_perm(n_row, n_grp, n_sub, bit):
    return [
        (index_of(n_row, n_grp, n_sub, q, g, r), index_of(n_row, n_grp, n_sub, q, g, r ^ bit))
        for q in range(n_row) for g in range(n_grp) for r in range(n_sub)
    ]


def gather_cols(block, perms):
    swap, far, near = perms
    sub = lax.axis_index("pr")
    high = sub // 2
    low = sub % 2
    mine = lax.ppermute(block, ALL, swap)
    other = lax.ppermute(mine, ALL, far)
    pair = jnp.where(high == 0, jnp.stack([mine, other]), jnp.stack([other, mine]))
    twin = lax.ppermute(pair, ALL, near)
    quad = jnp.where(low == 0, jnp.stack([pair, twin], 1), jnp.stack([twin, pair], 1))
    return quad.reshape((4,) + block.shape)


def row_sum(x):
    n = lax.axis_size("prow")
    q = lax.axis_index("prow")
    bits = [1 << b for b in range(n.bit_length() - 1)][::-1]
    seg = x
    for m in bits:
        half = seg.shape[0] // 2
        upper = (q // m) % 2 == 1
        keep = jnp.where(upper, seg[half:], seg[:half])
        send = jnp.where(upper, seg[:half], seg[half:])
        seg = keep + lax.ppermute(send, "prow", [(i, i ^ m) for i in range(n)])
    for m in bits[::-1]:
        upper = (q // m) % 2 == 1
        got = lax.ppermute(seg, "prow", [(i, i ^ m) for i in range(n)])
        seg = jnp.where(upper, jnp.concatenate([got, seg]), jnp.concatenate([seg, got]))
    return seg


def shards(ancestor_inv, tile_pattern, factor_block, row_blocks, diag_base):
    col_rows = ancestor_inv.shape[0]
    n_row = lax.axis_size("prow")
    n_grp = lax.axis_size("pg")
    n_sub = lax.axis_size("pr")
    perm = (
        swap_perm(n_row, n_grp, n_sub),
        flip_perm(n_row, n_grp, n_sub, 2),
        flip_perm(n_row, n_grp, n_sub, 1),
    )
    supers, _, kwidth = factor_block.shape
    pcol_idx = lax.axis_index("pg") * n_sub + lax.axis_index("pr")
    inverse_tiles = ancestor_inv * expand_tiles(tile_pattern)
    own_sel = structure_rows(row_blocks, pcol_idx * col_rows, col_rows)
    local_lower = factor_block * own_sel[:, :, None].astype(jnp.bfloat16)
    lower_cols = gather_cols(local_lower, perm)
    tiles4 = inverse_tiles.reshape(col_rows, n_sub, col_rows)
    partial = jnp.einsum(
        "irj,rsjk->sik", tiles4, lower_cols, preferred_element_type=jnp.float32
    )
    summed = lax.psum(partial, "prow")
    col_exact = -summed * own_sel[:, :, None]
    column = col_exact.astype(jnp.bfloat16)
    column_cols = gather_cols(column, perm)
    row_out = jnp.transpose(column_cols, (1, 3, 0, 2)).reshape(supers, kwidth, n_sub * col_rows)
    contrib = jnp.einsum(
        "rsjk,rsjl->skl", lower_cols, column_cols, preferred_element_type=jnp.float32
    )
    flat = contrib.reshape(supers * kwidth, kwidth)
    diagonal = diag_base - row_sum(flat).reshape(supers, kwidth, kwidth)
    return (column, row_out, diagonal)


def solution(mesh):
    n_row, n_col = mesh.devices.shape
    n_sub = n_col // n_row
    split = Mesh(mesh.devices.reshape(n_row, n_row, n_sub), ALL)
    in_specs = (P(COLS, "prow"), P(COLS, "prow"), P(None, COLS, None), P(), P())
    out_specs = (P(None, COLS, None), P(None, None, "prow"), P())
    return jax.shard_map(shards, mesh=split, in_specs=in_specs, out_specs=out_specs, check_vma=False)
```

```python
import jax
import jax.numpy as jnp
from jax import lax
from jax.sharding import Mesh
from jax.sharding import PartitionSpec as P

BLK = 128
COLS = ("pg", "pr")
ALL = ("prow", "pg", "pr")


def expand_tiles(pattern):
    tile_rows, tile_cols = pattern.shape
    widened = jnp.broadcast_to(
        pattern.astype(jnp.bfloat16)[:, None, :, None], (tile_rows, BLK, tile_cols, BLK)
    )
    return widened.reshape(tile_rows * BLK, tile_cols * BLK)


def structure_rows(row_blocks, row_start, how_many):
    row_ids = row_start + jnp.arange(how_many, dtype=jnp.int32)
    matches = row_blocks[:, None, :] == (row_ids // BLK)[None, :, None]
    return jnp.any(matches, axis=2).astype(jnp.float32)


def index_of(n_row, n_grp, n_sub, q, g, r):
    return (q * n_grp + g) * n_sub + r


def skew(q, g, n_row):
    side = 4 if n_row % 4 == 0 else 1
    return q - q % side + (g + q) % side


def swap_perm(n_row, n_grp, n_sub):
    return [
        (index_of(n_row, n_grp, n_sub, q, g, r), index_of(n_row, n_grp, n_sub, g, skew(q, g, n_row), r))
        for q in range(n_row) for g in range(n_grp) for r in range(n_sub)
    ]


def flip_perm(n_row, n_grp, n_sub, bit):
    return [
        (index_of(n_row, n_grp, n_sub, q, g, r), index_of(n_row, n_grp, n_sub, q, g, r ^ bit))
        for q in range(n_row) for g in range(n_grp) for r in range(n_sub)
    ]


def gather_cols(block, perms):
    swap, far, near = perms
    sub = lax.axis_index("pr")
    high = sub // 2
    low = sub % 2
    mine = lax.ppermute(block, ALL, swap)
    other = lax.ppermute(mine, ALL, far)
    pair = jnp.where(high == 0, jnp.stack([mine, other]), jnp.stack([other, mine]))
    twin = lax.ppermute(pair, ALL, near)
    quad = jnp.where(low == 0, jnp.stack([pair, twin], 1), jnp.stack([twin, pair], 1))
    return quad.reshape((4,) + block.shape)


def row_sum(x, order=None, between=None):
    n = lax.axis_size("prow")
    q = lax.axis_index("prow")
    bits = order or [1 << b for b in range(n.bit_length() - 1)][::-1]
    seg = x
    for m in bits:
        half = seg.shape[0] // 2
        upper = (q // m) % 2 == 1
        keep = jnp.where(upper, seg[half:], seg[:half])
        send = jnp.where(upper, seg[:half], seg[half:])
        seg = keep + lax.ppermute(send, "prow", [(i, i ^ m) for i in range(n)])
    if between is not None:
        seg = between(seg)
    for m in bits[::-1]:
        upper = (q // m) % 2 == 1
        got = lax.ppermute(seg, "prow", [(i, i ^ m) for i in range(n)])
        seg = jnp.where(upper, jnp.concatenate([got, seg]), jnp.concatenate([seg, got]))
    return seg


def shards(ancestor_inv, tile_pattern, factor_block, row_blocks, diag_base):
    col_rows = ancestor_inv.shape[0]
    n_row = lax.axis_size("prow")
    n_grp = lax.axis_size("pg")
    n_sub = lax.axis_size("pr")
    perm = (
        swap_perm(n_row, n_grp, n_sub),
        flip_perm(n_row, n_grp, n_sub, 2),
        flip_perm(n_row, n_grp, n_sub, 1),
    )
    supers, _, kwidth = factor_block.shape
    pcol_idx = lax.axis_index("pg") * n_sub + lax.axis_index("pr")
    inverse_tiles = ancestor_inv * expand_tiles(tile_pattern)
    own_sel = structure_rows(row_blocks, pcol_idx * col_rows, col_rows)
    local_lower = factor_block * own_sel[:, :, None].astype(jnp.bfloat16)
    lower_cols = gather_cols(local_lower, perm)
    tiles4 = inverse_tiles.reshape(col_rows, n_sub, col_rows)
    partial = jnp.einsum(
        "irj,rsjk->sik", tiles4, lower_cols, preferred_element_type=jnp.float32
    )
    n_row_bits = [1 << b for b in range(n_row.bit_length() - 1)]
    order = n_row_bits[-1:] + n_row_bits[:-1] if len(n_row_bits) == 3 else None
    summed = row_sum(
        partial.reshape(supers * col_rows, kwidth), order, lambda seg: seg.astype(jnp.bfloat16)
    ).reshape(supers, col_rows, kwidth)
    column = -summed * own_sel[:, :, None].astype(jnp.bfloat16)
    column_cols = gather_cols(column, perm)
    row_out = jnp.transpose(column_cols, (1, 3, 0, 2)).reshape(supers, kwidth, n_sub * col_rows)
    contrib = jnp.einsum(
        "rsjk,rsjl->skl", lower_cols, column_cols, preferred_element_type=jnp.float32
    )
    flat = contrib.reshape(supers * kwidth, kwidth)
    diagonal = diag_base - row_sum(flat).reshape(supers, kwidth, kwidth)
    return (column, row_out, diagonal)


def solution(mesh):
    n_row, n_col = mesh.devices.shape
    n_sub = n_col // n_row
    split = Mesh(mesh.devices.reshape(n_row, n_row, n_sub), ALL)
    in_specs = (P(COLS, "prow"), P(COLS, "prow"), P(None, COLS, None), P(), P())
    out_specs = (P(None, COLS, None), P(None, None, "prow"), P())
    return jax.shard_map(shards, mesh=split, in_specs=in_specs, out_specs=out_specs, check_vma=False)
```

```python
import jax
import jax.numpy as jnp
from jax import lax
from jax.sharding import Mesh
from jax.sharding import PartitionSpec as P

BLK = 128
COLS = ("pg", "pr")
ALL = ("prow", "pg", "pr")


def expand_tiles(pattern):
    tile_rows, tile_cols = pattern.shape
    widened = jnp.broadcast_to(
        pattern.astype(jnp.bfloat16)[:, None, :, None], (tile_rows, BLK, tile_cols, BLK)
    )
    return widened.reshape(tile_rows * BLK, tile_cols * BLK)


def structure_rows(row_blocks, row_start, how_many):
    row_ids = row_start + jnp.arange(how_many, dtype=jnp.int32)
    matches = row_blocks[:, None, :] == (row_ids // BLK)[None, :, None]
    return jnp.any(matches, axis=2).astype(jnp.float32)


def index_of(n_row, n_grp, n_sub, q, g, r):
    return (q * n_grp + g) * n_sub + r


def skew(q, g, n_row):
    side = 4 if n_row % 4 == 0 else 1
    return q - q % side + (g + q) % side


def swap_perm(n_row, n_grp, n_sub):
    return [
        (index_of(n_row, n_grp, n_sub, q, g, r), index_of(n_row, n_grp, n_sub, g, skew(q, g, n_row), r))
        for q in range(n_row) for g in range(n_grp) for r in range(n_sub)
    ]


def flip_perm(n_row, n_grp, n_sub, bit):
    return [
        (index_of(n_row, n_grp, n_sub, q, g, r), index_of(n_row, n_grp, n_sub, q, g, r ^ bit))
        for q in range(n_row) for g in range(n_grp) for r in range(n_sub)
    ]


def gather_cols(block, perms):
    swap, far, near = perms
    sub = lax.axis_index("pr")
    high = sub // 2
    low = sub % 2
    mine = lax.ppermute(block, ALL, swap)
    other = lax.ppermute(mine, ALL, far)
    pair = jnp.where(high == 0, jnp.stack([mine, other]), jnp.stack([other, mine]))
    twin = lax.ppermute(pair, ALL, near)
    quad = jnp.where(low == 0, jnp.stack([pair, twin], 1), jnp.stack([twin, pair], 1))
    return quad.reshape((4,) + block.shape)


def row_sum(x, order=None, between=None):
    n = lax.axis_size("prow")
    q = lax.axis_index("prow")
    bits = order or [1 << b for b in range(n.bit_length() - 1)][::-1]
    seg = x
    for m in bits:
        half = seg.shape[0] // 2
        upper = (q // m) % 2 == 1
        keep = jnp.where(upper, seg[half:], seg[:half])
        send = jnp.where(upper, seg[:half], seg[half:])
        seg = keep + lax.ppermute(send, "prow", [(i, i ^ m) for i in range(n)])
    if between is not None:
        seg = between(seg)
    for m in bits[::-1]:
        upper = (q // m) % 2 == 1
        got = lax.ppermute(seg, "prow", [(i, i ^ m) for i in range(n)])
        seg = jnp.where(upper, jnp.concatenate([got, seg]), jnp.concatenate([seg, got]))
    return seg


def shards(ancestor_inv, tile_pattern, factor_block, row_blocks, diag_base):
    col_rows = ancestor_inv.shape[0]
    n_row = lax.axis_size("prow")
    n_grp = lax.axis_size("pg")
    n_sub = lax.axis_size("pr")
    perm = (
        swap_perm(n_row, n_grp, n_sub),
        flip_perm(n_row, n_grp, n_sub, 2),
        flip_perm(n_row, n_grp, n_sub, 1),
    )
    supers, _, kwidth = factor_block.shape
    pcol_idx = lax.axis_index("pg") * n_sub + lax.axis_index("pr")
    inverse_tiles = ancestor_inv * expand_tiles(tile_pattern)
    own_sel = structure_rows(row_blocks, pcol_idx * col_rows, col_rows)
    local_lower = factor_block * own_sel[:, :, None].astype(jnp.bfloat16)
    lower_cols = gather_cols(local_lower, perm)
    lower_flat = jnp.transpose(lower_cols, (1, 0, 2, 3)).reshape(supers, n_sub * col_rows, kwidth)
    partial = jnp.einsum(
        "ij,sjk->sik", inverse_tiles, lower_flat, preferred_element_type=jnp.float32
    )
    n_row_bits = [1 << b for b in range(n_row.bit_length() - 1)]
    order = n_row_bits[-1:] + n_row_bits[:-1] if len(n_row_bits) == 3 else None
    summed = row_sum(
        partial.reshape(supers * col_rows, kwidth), order, lambda seg: seg.astype(jnp.bfloat16)
    ).reshape(supers, col_rows, kwidth)
    column = -summed * own_sel[:, :, None].astype(jnp.bfloat16)
    column_cols = gather_cols(column, perm)
    row_out = jnp.transpose(column_cols, (1, 3, 0, 2)).reshape(supers, kwidth, n_sub * col_rows)
    contrib = jnp.einsum(
        "rsjk,rsjl->skl", lower_cols, column_cols, preferred_element_type=jnp.float32
    )
    flat = contrib.reshape(supers * kwidth, kwidth)
    diagonal = diag_base - row_sum(flat).reshape(supers, kwidth, kwidth)
    return (column, row_out, diagonal)


def solution(mesh):
    n_row, n_col = mesh.devices.shape
    n_sub = n_col // n_row
    split = Mesh(mesh.devices.reshape(n_row, n_row, n_sub), ALL)
    in_specs = (P(COLS, "prow"), P(COLS, "prow"), P(None, COLS, None), P(), P())
    out_specs = (P(None, COLS, None), P(None, None, "prow"), P())
    return jax.shard_map(shards, mesh=split, in_specs=in_specs, out_specs=out_specs, check_vma=False)
```

```python
import jax
import jax.numpy as jnp
from jax import lax
from jax.sharding import Mesh
from jax.sharding import PartitionSpec as P

BLK = 128
COLS = ("pg", "pr")
ALL = ("prow", "pg", "pr")


def expand_tiles(pattern):
    tile_rows, tile_cols = pattern.shape
    widened = jnp.broadcast_to(
        pattern.astype(jnp.bfloat16)[:, None, :, None], (tile_rows, BLK, tile_cols, BLK)
    )
    return widened.reshape(tile_rows * BLK, tile_cols * BLK)


def structure_rows(row_blocks, row_start, how_many):
    row_ids = row_start + jnp.arange(how_many, dtype=jnp.int32)
    matches = row_blocks[:, None, :] == (row_ids // BLK)[None, :, None]
    return jnp.any(matches, axis=2).astype(jnp.float32)


def index_of(n_row, n_grp, n_sub, q, g, r):
    return (q * n_grp + g) * n_sub + r


def skew(q, g, n_row):
    side = 4 if n_row % 4 == 0 else 1
    return q - q % side + (g + q) % side


def swap_perm(n_row, n_grp, n_sub):
    return [
        (index_of(n_row, n_grp, n_sub, q, g, r), index_of(n_row, n_grp, n_sub, g, skew(q, g, n_row), r))
        for q in range(n_row) for g in range(n_grp) for r in range(n_sub)
    ]


def flip_perm(n_row, n_grp, n_sub, bit):
    return [
        (index_of(n_row, n_grp, n_sub, q, g, r), index_of(n_row, n_grp, n_sub, q, g, r ^ bit))
        for q in range(n_row) for g in range(n_grp) for r in range(n_sub)
    ]


def gather_cols(block, perms, axis=0):
    swap, far, near = perms
    sub = lax.axis_index("pr")
    high = sub // 2
    low = sub % 2
    mine = lax.ppermute(block, ALL, swap)
    other = lax.ppermute(mine, ALL, far)
    pair = jnp.where(high == 0, jnp.stack([mine, other], axis), jnp.stack([other, mine], axis))
    twin = lax.ppermute(pair, ALL, near)
    return jnp.where(low == 0, jnp.stack([pair, twin], axis + 1), jnp.stack([twin, pair], axis + 1))


def row_sum(x, order=None, between=None):
    n = lax.axis_size("prow")
    q = lax.axis_index("prow")
    bits = order or [1 << b for b in range(n.bit_length() - 1)][::-1]
    seg = x
    for m in bits:
        half = seg.shape[0] // 2
        upper = (q // m) % 2 == 1
        keep = jnp.where(upper, seg[half:], seg[:half])
        send = jnp.where(upper, seg[:half], seg[half:])
        seg = keep + lax.ppermute(send, "prow", [(i, i ^ m) for i in range(n)])
    if between is not None:
        seg = between(seg)
    for m in bits[::-1]:
        upper = (q // m) % 2 == 1
        got = lax.ppermute(seg, "prow", [(i, i ^ m) for i in range(n)])
        seg = jnp.where(upper, jnp.concatenate([got, seg]), jnp.concatenate([seg, got]))
    return seg


def shards(ancestor_inv, tile_pattern, factor_block, row_blocks, diag_base):
    col_rows = ancestor_inv.shape[0]
    n_row = lax.axis_size("prow")
    n_grp = lax.axis_size("pg")
    n_sub = lax.axis_size("pr")
    perm = (
        swap_perm(n_row, n_grp, n_sub),
        flip_perm(n_row, n_grp, n_sub, 2),
        flip_perm(n_row, n_grp, n_sub, 1),
    )
    supers, _, kwidth = factor_block.shape
    pcol_idx = lax.axis_index("pg") * n_sub + lax.axis_index("pr")
    inverse_tiles = ancestor_inv * expand_tiles(tile_pattern)
    own_sel = structure_rows(row_blocks, pcol_idx * col_rows, col_rows)
    local_lower = factor_block * own_sel[:, :, None].astype(jnp.bfloat16)
    lower_cols = gather_cols(local_lower, perm).reshape((n_sub,) + local_lower.shape)
    lower_flat = jnp.transpose(lower_cols, (1, 0, 2, 3)).reshape(supers, n_sub * col_rows, kwidth)
    partial = jnp.einsum(
        "ij,sjk->sik", inverse_tiles, lower_flat, preferred_element_type=jnp.float32
    )
    n_row_bits = [1 << b for b in range(n_row.bit_length() - 1)]
    order = n_row_bits[-1:] + n_row_bits[:-1] if len(n_row_bits) == 3 else None
    summed = row_sum(
        partial.reshape(supers * col_rows, kwidth), order, lambda seg: seg.astype(jnp.bfloat16)
    ).reshape(supers, col_rows, kwidth)
    column = -summed * own_sel[:, :, None].astype(jnp.bfloat16)
    column_rows = gather_cols(jnp.swapaxes(column, 1, 2), perm, 2)
    row_out = column_rows.reshape(supers, kwidth, n_sub * col_rows)
    contrib = jnp.einsum(
        "tsjk,sltj->skl",
        lower_cols,
        column_rows.reshape(supers, kwidth, n_sub, col_rows),
        preferred_element_type=jnp.float32,
    )
    flat = contrib.reshape(supers * kwidth, kwidth)
    diagonal = diag_base - row_sum(flat).reshape(supers, kwidth, kwidth)
    return (column, row_out, diagonal)


def solution(mesh):
    n_row, n_col = mesh.devices.shape
    n_sub = n_col // n_row
    split = Mesh(mesh.devices.reshape(n_row, n_row, n_sub), ALL)
    in_specs = (P(COLS, "prow"), P(COLS, "prow"), P(None, COLS, None), P(), P())
    out_specs = (P(None, COLS, None), P(None, None, "prow"), P())
    return jax.shard_map(shards, mesh=split, in_specs=in_specs, out_specs=out_specs, check_vma=False)
```

```python
import jax
import jax.numpy as jnp
from jax import lax
from jax.sharding import Mesh
from jax.sharding import PartitionSpec as P

BLK = 128
COLS = ("pg", "pr")
ALL = ("prow", "pg", "pr")


def expand_tiles(pattern):
    tile_rows, tile_cols = pattern.shape
    widened = jnp.broadcast_to(
        pattern.astype(jnp.bfloat16)[:, None, :, None], (tile_rows, BLK, tile_cols, BLK)
    )
    return widened.reshape(tile_rows * BLK, tile_cols * BLK)


def structure_rows(row_blocks, row_start, how_many):
    row_ids = row_start + jnp.arange(how_many, dtype=jnp.int32)
    matches = row_blocks[:, None, :] == (row_ids // BLK)[None, :, None]
    return jnp.any(matches, axis=2).astype(jnp.float32)


def index_of(n_row, n_grp, n_sub, q, g, r):
    return (q * n_grp + g) * n_sub + r


def skew(q, g, n_row):
    side = 4 if n_row % 4 == 0 else 1
    return q - q % side + (g + q) % side


def swap_perm(n_row, n_grp, n_sub):
    return [
        (index_of(n_row, n_grp, n_sub, q, g, r), index_of(n_row, n_grp, n_sub, g, skew(q, g, n_row), r))
        for q in range(n_row) for g in range(n_grp) for r in range(n_sub)
    ]


def flip_perm(n_row, n_grp, n_sub, bit):
    return [
        (index_of(n_row, n_grp, n_sub, q, g, r), index_of(n_row, n_grp, n_sub, q, g, r ^ bit))
        for q in range(n_row) for g in range(n_grp) for r in range(n_sub)
    ]


def gather_cols(block, perms):
    swap, far, near = perms
    sub = lax.axis_index("pr")
    high = sub // 2
    low = sub % 2
    mine = lax.ppermute(block, ALL, swap)
    other = lax.ppermute(mine, ALL, far)
    pair = jnp.where(high == 0, jnp.stack([mine, other]), jnp.stack([other, mine]))
    twin = lax.ppermute(pair, ALL, near)
    quad = jnp.where(low == 0, jnp.stack([pair, twin], 1), jnp.stack([twin, pair], 1))
    return quad.reshape((4,) + block.shape)


def row_sum(x, order=None, between=None):
    n = lax.axis_size("prow")
    q = lax.axis_index("prow")
    bits = order or [1 << b for b in range(n.bit_length() - 1)][::-1]
    seg = x
    for m in bits:
        half = seg.shape[0] // 2
        upper = (q // m) % 2 == 1
        keep = jnp.where(upper, seg[half:], seg[:half])
        send = jnp.where(upper, seg[:half], seg[half:])
        seg = keep + lax.ppermute(send, "prow", [(i, i ^ m) for i in range(n)])
    if between is not None:
        seg = between(seg)
    for m in bits[::-1]:
        upper = (q // m) % 2 == 1
        got = lax.ppermute(seg, "prow", [(i, i ^ m) for i in range(n)])
        seg = jnp.where(upper, jnp.concatenate([got, seg]), jnp.concatenate([seg, got]))
    return seg


def shards(ancestor_inv, tile_pattern, factor_block, row_blocks, diag_base):
    col_rows = ancestor_inv.shape[0]
    n_row = lax.axis_size("prow")
    n_grp = lax.axis_size("pg")
    n_sub = lax.axis_size("pr")
    perm = (
        swap_perm(n_row, n_grp, n_sub),
        flip_perm(n_row, n_grp, n_sub, 2),
        flip_perm(n_row, n_grp, n_sub, 1),
    )
    supers, _, kwidth = factor_block.shape
    pcol_idx = lax.axis_index("pg") * n_sub + lax.axis_index("pr")
    inverse_tiles = ancestor_inv * expand_tiles(tile_pattern)
    own_sel = structure_rows(row_blocks, pcol_idx * col_rows, col_rows)
    local_lower = factor_block * own_sel[:, :, None].astype(jnp.bfloat16)
    lower_cols = gather_cols(local_lower, perm)
    lower_flat = jnp.transpose(lower_cols, (1, 0, 2, 3)).reshape(supers, n_sub * col_rows, kwidth)
    partial = jnp.einsum(
        "ij,sjk->sik", inverse_tiles, lower_flat, preferred_element_type=jnp.float32
    )
    n_row_bits = [1 << b for b in range(n_row.bit_length() - 1)]
    order = n_row_bits[-1:] + n_row_bits[:-1] if len(n_row_bits) == 3 else None
    summed = row_sum(
        partial.reshape(supers * col_rows, kwidth), order, lambda seg: seg.astype(jnp.bfloat16)
    ).reshape(supers, col_rows, kwidth)
    column = -summed * own_sel[:, :, None].astype(jnp.bfloat16)
    column_cols = gather_cols(column, perm)
    row_out = jnp.transpose(column_cols, (1, 3, 0, 2)).reshape(supers, kwidth, n_sub * col_rows)
    contrib = jnp.einsum(
        "rsjk,rsjl->skl", lower_cols, column_cols, preferred_element_type=jnp.float32
    )
    flat = contrib.reshape(supers * kwidth, kwidth)
    diagonal = diag_base - row_sum(flat, order).reshape(supers, kwidth, kwidth)
    return (column, row_out, diagonal)


def solution(mesh):
    n_row, n_col = mesh.devices.shape
    n_sub = n_col // n_row
    split = Mesh(mesh.devices.reshape(n_row, n_row, n_sub), ALL)
    in_specs = (P(COLS, "prow"), P(COLS, "prow"), P(None, COLS, None), P(), P())
    out_specs = (P(None, COLS, None), P(None, None, "prow"), P())
    return jax.shard_map(shards, mesh=split, in_specs=in_specs, out_specs=out_specs, check_vma=False)
```
